32 devices in a mesh: rep: 8 (over z, y), tp: 4 (over x, core).
Axes of the slice: x: 2, y: 2, z: 4, core: 2. Of those that a mesh axis runs over, the one named last changes fastest.
Arguments:
- value_weight: bfloat16 [8, 2, 2048, 2048], P('rep', None, None, 'tp'), may hold values from -0.125 to 0.125
- output_weight: bfloat16 [8, 2, 2048, 2048], P('rep', None, 'tp'), may hold values from -0.125 to 0.125
- value_tracker: bfloat16 [8, 2, 2048, 2048], P('rep', None, None, 'tp'), may hold values from -6 to 6
- output_tracker: bfloat16 [8, 2, 2048, 2048], P('rep', None, 'tp'), may hold values from -6 to 6
- value_grad_prev: bfloat16 [8, 2, 2048, 2048], P('rep', None, None, 'tp'), may hold values from -6 to 6
- output_grad_prev: bfloat16 [8, 2, 2048, 2048], P('rep', None, 'tp'), may hold values from -6 to 6
- byte_ids: int32 [8, 1024], P('rep', 'tp'), may hold values from 0 to 255
- embed_table: bfloat16 [256, 2048], replicated, may hold values from -6 to 6
- decay_rate: float32 [2, 2048], P(None, 'tp'), may hold values from 0.003 to 0.2
- out_cotangent: bfloat16 [8, 1024, 2048], P('rep', 'tp'), may hold values from -0.29882812 to 0.29882812
- step_index: int32 [1], replicated, may hold values from 0 to 63
Outputs:
- new_value_weight: bfloat16 [8, 2, 2048, 2048], P('rep', None, None, 'tp')
- new_output_weight: bfloat16 [8, 2, 2048, 2048], P('rep', None, 'tp')
- new_value_tracker: bfloat16 [8, 2, 2048, 2048], P('rep', None, None, 'tp')
- new_output_tracker: bfloat16 [8, 2, 2048, 2048], P('rep', None, 'tp')
The draws below stay inside these ranges and needn't reach their ends.
All inputs are finite; a program needn't handle non-finite values.
Results may differ from the reference program's by a relative error of at most 0.004.
Values may be sent and summed in bfloat16 or wider, within the bound.
No kernel may reach another device: no remote copies, remote signals or barrier semaphores. Data moves between devices by JAX's collectives and lax.ppermute only.
A program may use at most 128 MiB of HBM per device.

```python
import math
import jax
import jax.numpy as jnp
import numpy as np
from jax import lax

D = 2048
H = 2048
VOCAB = 256
LAYERS = 2
SEQ_LEN = 1024
REPLICAS = 8
HOPS = 3
N_REP = 8
N_TP = 4


def place_ends(values, key, least, high):
    index_at = [jax.random.randint(jax.random.fold_in(key, axis), (), 0, length) for axis, length in enumerate(values.shape)]
    main_axis = values.shape.index(max(values.shape))
    beside = index_at[:main_axis] + [(index_at[main_axis] + 1) % values.shape[main_axis]] + index_at[main_axis + 1:]
    return values.at[tuple(index_at)].set(least).at[tuple(beside)].set(high)


def levels(stream_key, shape, shards, least, largest):
    level = 1.0
    for dim, parts in shards:
        heights = jax.random.uniform(jax.random.fold_in(jax.random.fold_in(stream_key, 6), dim), (parts,), jnp.float32, least / len(shards), largest / len(shards))
        level = level * jnp.repeat(jnp.exp(heights), shape[dim] // parts).reshape((-1,) + (1,) * (len(shape) - 1 - dim))
    return level


def rank_table(amount, skew):
    portions = [(1 << 20) // math.isqrt(standing ** skew) + 1 for standing in range(1, amount + 1)]
    spread = 1 + sum(portions) // (1 << 30)
    return np.cumsum(np.array([max(1, weight // spread) for weight in portions]))


def ranked_ids(key, extent, number_of, skew):
    listing = rank_table(number_of, skew)
    pick = jax.random.randint(jax.random.fold_in(key, 1), extent, 0, int(listing[number_of - 1]))
    standing = jnp.searchsorted(jnp.asarray(listing, jnp.int32), pick, side="right")
    return jax.random.permutation(jax.random.fold_in(key, 2), number_of)[standing].astype(jnp.int32)


def gaussian(rng, extent, spread, reach, split=(), held_as=jnp.bfloat16):
    values = spread * jax.random.normal(rng, extent, jnp.float32)
    if split:
        values = values * levels(rng, extent, split, -0.22, 0.18)
    return jnp.clip(values, -reach, reach).astype(held_as)


def setup_inputs(seed: int = 0) -> dict:
    key_list = jax.random.split(jax.random.key(seed), 12)
    value_weight = gaussian(key_list[0], (REPLICAS, LAYERS, D, H), D ** -0.5, 0.125, ((0, 8), (3, 4)))
    output_weight = gaussian(key_list[1], (REPLICAS, LAYERS, H, D), H ** -0.5, 0.125, ((0, 8), (2, 4)))
    value_tracker = gaussian(key_list[2], (REPLICAS, LAYERS, D, H), 1.0, 6.0, ((0, 8), (3, 4)))
    output_tracker = gaussian(key_list[3], (REPLICAS, LAYERS, H, D), 1.0, 6.0, ((0, 8), (2, 4)))
    value_grad_prev = gaussian(key_list[4], (REPLICAS, LAYERS, D, H), 1.0, 6.0, ((0, 8), (3, 4)))
    output_grad_prev = gaussian(key_list[5], (REPLICAS, LAYERS, H, D), 1.0, 6.0, ((0, 8), (2, 4)))
    byte_ids = place_ends(ranked_ids(key_list[6], (REPLICAS, SEQ_LEN), VOCAB, 2), jax.random.fold_in(key_list[6], 3), 0, VOCAB - 1).astype(jnp.int32)
    embed_table = gaussian(key_list[7], (VOCAB, D), 1.0, 6.0)
    decay_rate = jnp.clip(jnp.exp(math.log(0.2) - 4.199705 * jax.random.uniform(key_list[8], (LAYERS, H), jnp.float32) ** levels(key_list[8], (LAYERS, H), ((1, 4),), -0.2, 0.2)), 0.003, 0.2)
    out_cotangent = gaussian(key_list[9], (REPLICAS, SEQ_LEN, D), 0.05, 0.29882812, ((0, 8), (1, 4)))
    step_index = jax.random.randint(key_list[10], (1,), 0, 64).astype(jnp.int32)
    return dict(value_weight=value_weight, output_weight=output_weight, value_tracker=value_tracker, output_tracker=output_tracker, value_grad_prev=value_grad_prev, output_grad_prev=output_grad_prev, byte_ids=byte_ids, embed_table=embed_table, decay_rate=decay_rate, out_cotangent=out_cotangent, step_index=step_index)


norm_eps = 1e-05
rate_step = 0.02

def scan_join(earlier, later_part):
    return (earlier[0] * later_part[0], later_part[0] * earlier[1] + later_part[1])

def causal_mix(values, keep_rate):
    decay_coeff = jnp.broadcast_to(keep_rate, values.shape)
    return lax.associative_scan(scan_join, (decay_coeff, (1.0 - keep_rate) * values), axis=0)[1]

def causal_back(grad_values, keep_rate):
    decay_coeff = jnp.broadcast_to(keep_rate, grad_values.shape)
    summed = lax.associative_scan(scan_join, (decay_coeff, grad_values), axis=0, reverse=True)[1]
    return (1.0 - keep_rate) * summed

def norm_rows(hidden):
    hidden_wide = hidden.astype(jnp.float32)
    inv_scale = lax.rsqrt(lax.optimization_barrier(jnp.mean(hidden_wide * hidden_wide, axis=-1, keepdims=True)) + norm_eps)
    return (hidden_wide, inv_scale, (hidden_wide * inv_scale).astype(jnp.bfloat16))

def norm_back(hidden_wide, inv_scale, grad_norm):
    mean_term = lax.optimization_barrier(jnp.mean(hidden_wide * grad_norm, axis=-1, keepdims=True))
    return inv_scale * grad_norm - hidden_wide * inv_scale * inv_scale * inv_scale * mean_term

def group_sum(left_mat, right_mat, groups):
    row_count = left_mat.shape[0]
    inner_width = left_mat.shape[1] // groups
    left_three = left_mat.astype(jnp.float32).reshape(row_count, groups, inner_width)
    right_three = right_mat.astype(jnp.float32).reshape(groups, inner_width, right_mat.shape[1])
    partials = jnp.einsum('tgk,gkd->gtd', left_three, right_three)
    partials = lax.optimization_barrier(partials.astype(jnp.bfloat16))
    return lax.optimization_barrier(jnp.sum(partials.astype(jnp.float32), axis=0))

def replica_grads(value_mats, output_mats, byte_row, embed_table, keep_all, cotangent):
    onehot = (byte_row[:, None] == jnp.arange(VOCAB, dtype=jnp.int32)[None, :]).astype(jnp.bfloat16)
    hidden = jnp.dot(onehot, embed_table, preferred_element_type=jnp.float32).astype(jnp.bfloat16)
    saved = []
    for layer_idx in range(LAYERS):
        hidden_wide, inv_scale, normed = norm_rows(hidden)
        mixin = jnp.dot(normed, value_mats[layer_idx], preferred_element_type=jnp.float32)
        scan_state = causal_mix(mixin, keep_all[layer_idx])
        gated_act = jax.nn.silu(scan_state).astype(jnp.bfloat16)
        saved.append((hidden_wide, inv_scale, normed, scan_state, gated_act))
        if layer_idx + 1 < LAYERS:
            branch = group_sum(gated_act, output_mats[layer_idx], N_TP)
            hidden = (hidden.astype(jnp.float32) + branch).astype(jnp.bfloat16)
    grad_hidden = cotangent
    value_list = [None] * LAYERS
    output_list = [None] * LAYERS
    for layer_idx in reversed(range(LAYERS)):
        hidden_wide, inv_scale, normed, scan_state, gated_act = saved[layer_idx]
        grad_act = jnp.dot(grad_hidden, output_mats[layer_idx].T, preferred_element_type=jnp.float32)
        output_list[layer_idx] = jnp.dot(gated_act.T, grad_hidden, preferred_element_type=jnp.float32)
        sigmoid_s = jax.nn.sigmoid(scan_state)
        grad_state = grad_act * sigmoid_s * (1.0 + scan_state * (1.0 - sigmoid_s))
        grad_in = causal_back(grad_state, keep_all[layer_idx]).astype(jnp.bfloat16)
        value_list[layer_idx] = jnp.dot(normed.T, grad_in, preferred_element_type=jnp.float32)
        if layer_idx > 0:
            grad_norm = group_sum(grad_in, value_mats[layer_idx].T, N_TP)
            grad_hidden = (grad_hidden.astype(jnp.float32) + norm_back(hidden_wide, inv_scale, grad_norm)).astype(jnp.bfloat16)
    return (jnp.stack(value_list), jnp.stack(output_list))

def mix_update(weight, tracker, previous, gradient, partner):
    new_tracker = 0.5 * (tracker.astype(jnp.float32) + tracker[partner].astype(jnp.float32)) + gradient - previous.astype(jnp.float32)
    new_weight = 0.5 * (weight.astype(jnp.float32) + weight[partner].astype(jnp.float32)) - rate_step * new_tracker
    return (new_weight.astype(jnp.bfloat16), new_tracker.astype(jnp.bfloat16))

def reference(value_weight, output_weight, value_tracker, output_tracker, value_grad_prev, output_grad_prev, byte_ids, embed_table, decay_rate, out_cotangent, step_index):
    keep_all = jnp.exp(-decay_rate)
    value_grads = []
    output_grads = []
    for replica in range(N_REP):
        value_g, output_g = replica_grads(value_weight[replica], output_weight[replica], byte_ids[replica], embed_table, keep_all, out_cotangent[replica])
        value_grads.append(value_g)
        output_grads.append(output_g)
    value_grad = jnp.stack(value_grads)
    output_grad = jnp.stack(output_grads)
    swap_bit = (step_index[0] % HOPS).astype(jnp.int32)
    partner = jnp.bitwise_xor(jnp.arange(N_REP, dtype=jnp.int32), jnp.left_shift(jnp.int32(1), swap_bit).astype(jnp.int32))
    new_value_weight, new_value_tracker = mix_update(value_weight, value_tracker, value_grad_prev, value_grad, partner)
    new_output_weight, new_output_tracker = mix_update(output_weight, output_tracker, output_grad_prev, output_grad, partner)
    return (new_value_weight, new_output_weight, new_value_tracker, new_output_tracker)
```

```python
from functools import partial

import jax
import jax.numpy as jnp
from jax import lax
from jax.sharding import PartitionSpec as P

norm_eps = 1e-05
rate_step = 0.02


def shortened(x):

    def short(part):
        return part.astype(jnp.bfloat16) if part.dtype == jnp.float32 else part

    return jax.tree.map(short, x)


def from_partner(x, axis, bit):
    return lax.ppermute(x, axis, [(i, i ^ 1 << bit) for i in range(lax.axis_size(axis))])


def scan_join(earlier, later_part):
    return (earlier[0] * later_part[0], later_part[0] * earlier[1] + later_part[1])


def causal_mix(values, keep_rate):
    decay_coeff = jnp.broadcast_to(keep_rate, values.shape)
    return lax.associative_scan(scan_join, (decay_coeff, (1.0 - keep_rate) * values), axis=0)[1]


def causal_back(grad_values, keep_rate):
    decay_coeff = jnp.broadcast_to(keep_rate, grad_values.shape)
    summed = lax.associative_scan(scan_join, (decay_coeff, grad_values), axis=0, reverse=True)[1]
    return (1.0 - keep_rate) * summed


def norm_rows(hidden):
    hidden_wide = hidden.astype(jnp.float32)
    inv_scale = lax.rsqrt(jnp.mean(hidden_wide * hidden_wide, axis=-1, keepdims=True) + norm_eps)
    return (hidden_wide, inv_scale, (hidden_wide * inv_scale).astype(jnp.bfloat16))


def norm_back(hidden_wide, inv_scale, grad_norm):
    mean_term = jnp.mean(hidden_wide * grad_norm, axis=-1, keepdims=True)
    return inv_scale * grad_norm - hidden_wide * inv_scale * inv_scale * inv_scale * mean_term


def embed_rows(byte_row, embed_table):
    vocab_size = embed_table.shape[0]
    onehot = (byte_row[:, None] == jnp.arange(vocab_size, dtype=jnp.int32)[None, :]).astype(
        jnp.bfloat16
    )
    return jnp.dot(onehot, embed_table, preferred_element_type=jnp.float32).astype(jnp.bfloat16)


def trade_whole(payload, bit_number):
    return from_partner(
        (
            shortened(payload[0]),
            shortened(payload[1]),
            shortened(payload[2]),
            shortened(payload[3]),
        ),
        "rep",
        bit_number,
    )


def step_body(
    bit_number,
    value_weight,
    output_weight,
    value_tracker,
    output_tracker,
    value_grad_prev,
    output_grad_prev,
    byte_ids,
    embed_table,
    decay_rate,
    out_cotangent,
    step_index,
):
    layer_count = value_weight.shape[1]
    value_mats = value_weight[0]
    output_mats = output_weight[0]
    keep_all = jnp.exp(-decay_rate)
    partner_state = trade_whole(
        (value_weight, output_weight, value_tracker, output_tracker), bit_number
    )
    all_ids = lax.all_gather(byte_ids, "tp", axis=1, tiled=True)
    hidden = embed_rows(all_ids[0], embed_table)
    saved = []
    for layer_idx in range(layer_count):
        hidden_wide, inv_scale, normed = norm_rows(hidden)
        normed_full = normed
        mixin = jnp.dot(normed_full, value_mats[layer_idx], preferred_element_type=jnp.float32)
        scan_state = causal_mix(mixin, keep_all[layer_idx])
        gated_act = jax.nn.silu(scan_state).astype(jnp.bfloat16)
        saved.append((hidden_wide, inv_scale, normed_full, scan_state, gated_act))
        if layer_idx + 1 < layer_count:
            branch = lax.psum(
                jnp.dot(
                    gated_act, output_mats[layer_idx], preferred_element_type=jnp.float32
                ).astype(jnp.bfloat16),
                "tp",
            ).astype(jnp.float32)
            hidden = (hidden.astype(jnp.float32) + branch).astype(jnp.bfloat16)
    grad_hidden = lax.all_gather(out_cotangent[0], "tp", axis=0, tiled=True)
    value_list = [None] * layer_count
    output_list = [None] * layer_count
    for layer_idx in reversed(range(layer_count)):
        hidden_wide, inv_scale, normed_full, scan_state, gated_act = saved[layer_idx]
        grad_full = grad_hidden
        grad_act = jnp.dot(grad_full, output_mats[layer_idx].T, preferred_element_type=jnp.float32)
        output_list[layer_idx] = jnp.dot(gated_act.T, grad_full, preferred_element_type=jnp.float32)
        sigmoid_s = jax.nn.sigmoid(scan_state)
        grad_state = grad_act * sigmoid_s * (1.0 + scan_state * (1.0 - sigmoid_s))
        grad_in = causal_back(grad_state, keep_all[layer_idx]).astype(jnp.bfloat16)
        value_list[layer_idx] = jnp.dot(normed_full.T, grad_in, preferred_element_type=jnp.float32)
        if layer_idx > 0:
            grad_norm = lax.psum(
                jnp.dot(
                    grad_in, value_mats[layer_idx].T, preferred_element_type=jnp.float32
                ).astype(jnp.bfloat16),
                "tp",
            ).astype(jnp.float32)
            grad_hidden = (
                grad_hidden.astype(jnp.float32) + norm_back(hidden_wide, inv_scale, grad_norm)
            ).astype(jnp.bfloat16)
    value_grad = jnp.stack(value_list)[None]
    output_grad = jnp.stack(output_list)[None]
    other_value_w, other_output_w, other_value_t, other_output_t = partner_state
    value_track_new = (
        0.5 * (value_tracker.astype(jnp.float32) + other_value_t.astype(jnp.float32))
        + value_grad
        - value_grad_prev.astype(jnp.float32)
    )
    output_track_new = (
        0.5 * (output_tracker.astype(jnp.float32) + other_output_t.astype(jnp.float32))
        + output_grad
        - output_grad_prev.astype(jnp.float32)
    )
    value_weight_new = (
        0.5 * (value_weight.astype(jnp.float32) + other_value_w.astype(jnp.float32))
        - rate_step * value_track_new
    )
    output_weight_new = (
        0.5 * (output_weight.astype(jnp.float32) + other_output_w.astype(jnp.float32))
        - rate_step * output_track_new
    )
    return (
        value_weight_new.astype(jnp.bfloat16),
        output_weight_new.astype(jnp.bfloat16),
        value_track_new.astype(jnp.bfloat16),
        output_track_new.astype(jnp.bfloat16),
    )


def local(*args):
    step_index = args[-1]
    hop_count = lax.axis_size("rep").bit_length() - 1
    swap_bit = step_index[0] % hop_count
    branches = [partial(step_body, number) for number in range(hop_count)]
    return lax.switch(swap_bit, branches, *args)


def solution(mesh):
    in_specs = (
        P("rep", None, None, "tp"),
        P("rep", None, "tp", None),
        P("rep", None, None, "tp"),
        P("rep", None, "tp", None),
        P("rep", None, None, "tp"),
        P("rep", None, "tp", None),
        P("rep", "tp"),
        P(),
        P(None, "tp"),
        P("rep", "tp", None),
        P(),
    )
    out_specs = (
        P("rep", None, None, "tp"),
        P("rep", None, "tp", None),
        P("rep", None, None, "tp"),
        P("rep", None, "tp", None),
    )
    return jax.shard_map(local, mesh=mesh, in_specs=in_specs, out_specs=out_specs, check_vma=False)
```

```python
from functools import partial

import jax
import jax.numpy as jnp
from jax import lax
from jax.experimental import pallas as pl
from jax.experimental.pallas import tpu as pltpu
from jax.sharding import PartitionSpec as P

norm_eps = 1e-05
rate_step = 0.02


def shortened(x):

    def short(part):
        return part.astype(jnp.bfloat16) if part.dtype == jnp.float32 else part

    return jax.tree.map(short, x)


def from_partner(x, axis, bit):
    return lax.ppermute(x, axis, [(i, i ^ 1 << bit) for i in range(lax.axis_size(axis))])


TILE = 8
LANES = 128


def shift_down(a, d, fill):
    row = lax.broadcasted_iota(jnp.int32, a.shape, 0)
    return jnp.where(row >= d, pltpu.roll(a, d, 0), fill)


def shift_up(a, d, fill):
    row = lax.broadcasted_iota(jnp.int32, a.shape, 0)
    return jnp.where(row < TILE - d, pltpu.roll(a, TILE - d, 0), fill)


def keep_steps(keep_ref):
    kb = jnp.broadcast_to(keep_ref[...], (TILE, keep_ref.shape[1]))
    k2 = kb * kb
    return kb, {1: kb, 2: k2, 4: k2 * k2}


def mix_kernel(keep_ref, x_ref, state_ref, act_ref):
    kb, k_d = keep_steps(keep_ref)
    powers = kb
    for d in (1, 2, 4):
        powers = powers * shift_down(powers, d, 1.0)
    fresh = 1.0 - kb

    def body(t, carry):
        r = pl.multiple_of(t * TILE, TILE)
        acc = fresh * x_ref[pl.ds(r, TILE), :]
        for d in (1, 2, 4):
            acc = acc + k_d[d] * shift_down(acc, d, 0.0)
        s = acc + powers * carry
        state_ref[pl.ds(r, TILE), :] = s
        act_ref[pl.ds(r, TILE), :] = (s / (1.0 + jnp.exp(-s))).astype(act_ref.dtype)
        return s[TILE - 1 : TILE, :]

    lax.fori_loop(
        0, x_ref.shape[0] // TILE, body, jnp.zeros((1, x_ref.shape[1]), jnp.float32), unroll=4
    )


def back_kernel(keep_ref, ga_ref, s_ref, gin_ref):
    kb, k_d = keep_steps(keep_ref)
    powers = kb
    for d in (1, 2, 4):
        powers = powers * shift_up(powers, d, 1.0)
    fresh = 1.0 - kb
    n_tiles = ga_ref.shape[0] // TILE

    def body(t, carry):
        r = pl.multiple_of((n_tiles - 1 - t) * TILE, TILE)
        s = s_ref[pl.ds(r, TILE), :]
        sig = 1.0 / (1.0 + jnp.exp(-s))
        acc = ga_ref[pl.ds(r, TILE), :] * sig * (1.0 + s * (1.0 - sig))
        for d in (1, 2, 4):
            acc = acc + k_d[d] * shift_up(acc, d, 0.0)
        q = acc + powers * carry
        gin_ref[pl.ds(r, TILE), :] = (fresh * q).astype(gin_ref.dtype)
        return q[0:1, :]

    lax.fori_loop(0, n_tiles, body, jnp.zeros((1, ga_ref.shape[1]), jnp.float32), unroll=4)


def lane_specs(rows, count):
    return [pl.BlockSpec((rows, LANES), lambda j: (0, j)) for _ in range(count)]


def causal_mix(values, keep_rate):
    rows, cols = values.shape
    return pl.pallas_call(
        mix_kernel,
        grid=(cols // LANES,),
        in_specs=lane_specs(1, 1) + lane_specs(rows, 1),
        out_specs=lane_specs(rows, 2),
        out_shape=(
            jax.ShapeDtypeStruct((rows, cols), jnp.float32),
            jax.ShapeDtypeStruct((rows, cols), jnp.bfloat16),
        ),
    )(keep_rate.reshape(1, cols), values)


def causal_back(grad_act, scan_state, keep_rate):
    rows, cols = grad_act.shape
    return pl.pallas_call(
        back_kernel,
        grid=(cols // LANES,),
        in_specs=lane_specs(1, 1) + lane_specs(rows, 2),
        out_specs=lane_specs(rows, 1)[0],
        out_shape=jax.ShapeDtypeStruct((rows, cols), jnp.bfloat16),
    )(keep_rate.reshape(1, cols), grad_act, scan_state)


def norm_rows(hidden):
    hidden_wide = hidden.astype(jnp.float32)
    inv_scale = lax.rsqrt(jnp.mean(hidden_wide * hidden_wide, axis=-1, keepdims=True) + norm_eps)
    return (hidden_wide, inv_scale, (hidden_wide * inv_scale).astype(jnp.bfloat16))


def norm_back(hidden_wide, inv_scale, grad_norm):
    mean_term = jnp.mean(hidden_wide * grad_norm, axis=-1, keepdims=True)
    return inv_scale * grad_norm - hidden_wide * inv_scale * inv_scale * inv_scale * mean_term


def embed_rows(byte_row, embed_table):
    vocab_size = embed_table.shape[0]
    onehot = (byte_row[:, None] == jnp.arange(vocab_size, dtype=jnp.int32)[None, :]).astype(
        jnp.bfloat16
    )
    return jnp.dot(onehot, embed_table, preferred_element_type=jnp.float32).astype(jnp.bfloat16)


def trade_whole(payload, bit_number):
    return from_partner(
        (
            shortened(payload[0]),
            shortened(payload[1]),
            shortened(payload[2]),
            shortened(payload[3]),
        ),
        "rep",
        bit_number,
    )


def step_body(
    bit_number,
    value_weight,
    output_weight,
    value_tracker,
    output_tracker,
    value_grad_prev,
    output_grad_prev,
    byte_ids,
    embed_table,
    decay_rate,
    out_cotangent,
    step_index,
):
    layer_count = value_weight.shape[1]
    value_mats = value_weight[0]
    output_mats = output_weight[0]
    keep_all = jnp.exp(-decay_rate)
    partner_state = trade_whole(
        (value_weight, output_weight, value_tracker, output_tracker), bit_number
    )
    all_ids = lax.all_gather(byte_ids, "tp", axis=1, tiled=True)
    hidden = embed_rows(all_ids[0], embed_table)
    saved = []
    for layer_idx in range(layer_count):
        hidden_wide, inv_scale, normed = norm_rows(hidden)
        normed_full = normed
        mixin = jnp.dot(normed_full, value_mats[layer_idx], preferred_element_type=jnp.float32)
        scan_state, gated_act = causal_mix(mixin, keep_all[layer_idx])
        saved.append((hidden_wide, inv_scale, normed_full, scan_state, gated_act))
        if layer_idx + 1 < layer_count:
            branch = lax.psum(
                jnp.dot(
                    gated_act, output_mats[layer_idx], preferred_element_type=jnp.float32
                ).astype(jnp.bfloat16),
                "tp",
            ).astype(jnp.float32)
            hidden = (hidden.astype(jnp.float32) + branch).astype(jnp.bfloat16)
    grad_hidden = lax.all_gather(out_cotangent[0], "tp", axis=0, tiled=True)
    value_list = [None] * layer_count
    output_list = [None] * layer_count
    for layer_idx in reversed(range(layer_count)):
        hidden_wide, inv_scale, normed_full, scan_state, gated_act = saved[layer_idx]
        grad_full = grad_hidden
        grad_act = jnp.dot(grad_full, output_mats[layer_idx].T, preferred_element_type=jnp.float32)
        output_list[layer_idx] = jnp.dot(gated_act.T, grad_full, preferred_element_type=jnp.float32)
        grad_in = causal_back(grad_act, scan_state, keep_all[layer_idx])
        value_list[layer_idx] = jnp.dot(normed_full.T, grad_in, preferred_element_type=jnp.float32)
        if layer_idx > 0:
            grad_norm = lax.psum(
                jnp.dot(
                    grad_in, value_mats[layer_idx].T, preferred_element_type=jnp.float32
                ).astype(jnp.bfloat16),
                "tp",
            ).astype(jnp.float32)
            grad_hidden = (
                grad_hidden.astype(jnp.float32) + norm_back(hidden_wide, inv_scale, grad_norm)
            ).astype(jnp.bfloat16)
    value_grad = jnp.stack(value_list)[None]
    output_grad = jnp.stack(output_list)[None]
    other_value_w, other_output_w, other_value_t, other_output_t = partner_state
    value_track_new = (
        0.5 * (value_tracker.astype(jnp.float32) + other_value_t.astype(jnp.float32))
        + value_grad
        - value_grad_prev.astype(jnp.float32)
    )
    output_track_new = (
        0.5 * (output_tracker.astype(jnp.float32) + other_output_t.astype(jnp.float32))
        + output_grad
        - output_grad_prev.astype(jnp.float32)
    )
    value_weight_new = (
        0.5 * (value_weight.astype(jnp.float32) + other_value_w.astype(jnp.float32))
        - rate_step * value_track_new
    )
    output_weight_new = (
        0.5 * (output_weight.astype(jnp.float32) + other_output_w.astype(jnp.float32))
        - rate_step * output_track_new
    )
    return (
        value_weight_new.astype(jnp.bfloat16),
        output_weight_new.astype(jnp.bfloat16),
        value_track_new.astype(jnp.bfloat16),
        output_track_new.astype(jnp.bfloat16),
    )


def local(*args):
    step_index = args[-1]
    hop_count = lax.axis_size("rep").bit_length() - 1
    swap_bit = step_index[0] % hop_count
    branches = [partial(step_body, number) for number in range(hop_count)]
    return lax.switch(swap_bit, branches, *args)


def solution(mesh):
    in_specs = (
        P("rep", None, None, "tp"),
        P("rep", None, "tp", None),
        P("rep", None, None, "tp"),
        P("rep", None, "tp", None),
        P("rep", None, None, "tp"),
        P("rep", None, "tp", None),
        P("rep", "tp"),
        P(),
        P(None, "tp"),
        P("rep", "tp", None),
        P(),
    )
    out_specs = (
        P("rep", None, None, "tp"),
        P("rep", None, "tp", None),
        P("rep", None, None, "tp"),
        P("rep", None, "tp", None),
    )
    return jax.shard_map(local, mesh=mesh, in_specs=in_specs, out_specs=out_specs, check_vma=False)
```
